768 devices in a mesh: rep: 96 (over y_lo, z, core), fsdp: 8 (over y_hi, x).
Axes of the slice: x: 4, y: 8 (y_hi: 2, y_lo: 4; y = y_hi * 4 + y_lo), z: 12, core: 2. Of those that a mesh axis runs over, the one named last changes fastest.
Arguments:
- tokens: bfloat16 [393216, 2048], P(('rep', 'fsdp')), may hold values from -6 to 6
- out_grad: bfloat16 [393216, 256], P(('rep', 'fsdp')), may hold values from -6 to 6
- gain: float32 [96, 128], P('rep'), may hold values from 0.3 to 3
- inner_weight: float32 [96, 2048, 256], P('rep', 'fsdp'), may hold values from -6 to 6
- outer_weight: float32 [96, 2048, 256], P('rep', 'fsdp'), may hold values from -6.3 to 6.3
- momentum: float32 [96, 2048, 256], P('rep', 'fsdp'), may hold values from -1.2 to 1.2
- adam_m: float32 [96, 2048, 256], P('rep', 'fsdp'), may hold values from -2 to 2
- adam_v: float32 [96, 2048, 256], P('rep', 'fsdp'), may hold values from 0.5 to 8
- gossip_offset: int32 [1], replicated, may hold values from 0 to 65535
Outputs:
- outer_new: float32 [96, 2048, 256], P('rep', 'fsdp')
- momentum_new: float32 [96, 2048, 256], P('rep', 'fsdp')
- adam_m_new: float32 [96, 2048, 256], P('rep', 'fsdp')
- adam_v_new: float32 [96, 2048, 256], P('rep', 'fsdp')
The draws below stay inside these ranges and needn't reach their ends.
All inputs are finite; a program needn't handle non-finite values.
Results may differ from the reference program's by a relative error of at most 0.0038.
Values may be sent and summed in bfloat16 or wider, within the bound.
No kernel may reach another device: no remote copies, remote signals or barrier semaphores. Data moves between devices by JAX's collectives and lax.ppermute only.
A program may use at most 32 MiB of HBM per device.

```python
import math
import jax
import jax.numpy as jnp
from jax import lax

D = 2048
HEAD = 128
ADAM_STEP = 100
KV = 256
TOKENS = 393216
N_REP = 96


def paired_weights(key):
    folded = jax.random.fold_in(key, 4242)
    key_base, key_drift = jax.random.split(folded)
    full_shape = (N_REP, D, KV)
    base_weight = jnp.clip(jax.random.normal(key_base, full_shape, jnp.float32), -6.0, 6.0)
    drift = 0.05 * jnp.clip(jax.random.normal(key_drift, full_shape, jnp.float32), -4.0, 4.0)
    return (base_weight, base_weight + drift)


def draw_inner_weight(key, part):
    return paired_weights(key)[0]


def draw_outer_weight(key, part):
    return paired_weights(key)[1]


def shard_levels(own_key, extent, pieces, smallest, top_value):
    def one(axis_at, parts):
        draws = jax.random.uniform(jax.random.fold_in(jax.random.fold_in(own_key, 6), axis_at), (parts,), jnp.float32, smallest / len(pieces), top_value / len(pieces))
        return jnp.repeat(jnp.exp(draws), extent[axis_at] // parts).reshape((-1,) + (1,) * (len(extent) - axis_at - 1))

    level = one(*pieces[0])
    for cut in pieces[1:]:
        level = level * one(*cut)
    return level


def scatter_about(own_key, shape, spread, bound, pieces=(), kind=jnp.bfloat16):
    drawn = spread * jax.random.normal(own_key, shape, jnp.float32)
    if pieces:
        drawn = drawn * shard_levels(own_key, shape, pieces, -0.22, 0.18)
    return jnp.clip(drawn, -bound, bound).astype(kind)


def setup_inputs(seed: int = 0) -> dict:
    splits = jax.random.split(jax.random.key(seed), 10)
    return {
        "tokens": scatter_about(splits[0], (TOKENS, D), 1.0, 6.0, ((0, 768),)),
        "out_grad": scatter_about(splits[1], (TOKENS, KV), 1.0, 6.0, ((0, 768),)),
        "gain": jnp.clip(jnp.exp(math.log(3.0) - 2.3025851 * jax.random.uniform(splits[2], (N_REP, HEAD), jnp.float32) ** shard_levels(splits[2], (N_REP, HEAD), ((0, 96),), -0.2, 0.2)), 0.3, 3.0),
        "inner_weight": draw_inner_weight(jax.random.fold_in(splits[9], 71), 0),
        "outer_weight": draw_outer_weight(jax.random.fold_in(splits[9], 71), 0),
        "momentum": scatter_about(splits[5], (N_REP, D, KV), 0.2, 1.2, ((0, 96), (1, 8)), jnp.float32),
        "adam_m": scatter_about(splits[6], (N_REP, D, KV), 0.3, 2.0, ((0, 96), (1, 8)), jnp.float32),
        "adam_v": jnp.clip(jnp.exp(math.log(8.0) - 2.7725887 * jax.random.uniform(splits[7], (N_REP, D, KV), jnp.float32) ** shard_levels(splits[7], (N_REP, D, KV), ((0, 96), (1, 8)), -0.2, 0.2)), 0.5, 8.0),
        "gossip_offset": jax.random.randint(splits[8], (1,), 0, 65536).astype(jnp.int32),
    }


def replica_step(items):
    rows_x, rows_g, gain_row, inner, outer, first, second = items
    w_bf = inner.astype(jnp.bfloat16)
    keys = jnp.dot(rows_x, w_bf, preferred_element_type=jnp.float32)
    heads = keys.reshape(keys.shape[0], -1, HEAD)
    scale = lax.rsqrt(lax.optimization_barrier(jnp.mean(heads * heads, axis=-1, keepdims=True)) + 1e-06)
    unit = heads * scale
    g_out = rows_g.astype(jnp.float32).reshape(heads.shape) * gain_row
    inner_prod = lax.optimization_barrier(jnp.mean(unit * g_out, axis=-1, keepdims=True))
    key_grad = (scale * (g_out - unit * inner_prod)).reshape(keys.shape).astype(jnp.bfloat16)
    grad = jnp.dot(rows_x.T, key_grad, preferred_element_type=jnp.float32)
    first_new = 0.9 * first + 0.1 * grad
    second_new = 0.95 * second + 0.05 * grad * grad
    fix_one = 1.0 - 0.9 ** ADAM_STEP
    fix_two = 1.0 - 0.95 ** ADAM_STEP
    update = first_new / fix_one / (jnp.sqrt(second_new / fix_two) + 1e-08) + 0.1 * inner
    inner_next = inner - 0.05 * update
    delta = outer - inner_next
    return (first_new, second_new, delta)

def reference(tokens, out_grad, gain, inner_weight, outer_weight, momentum, adam_m, adam_v, gossip_offset):
    per_rep = tokens.shape[0] // N_REP
    rows_x = tokens.reshape(N_REP, per_rep, tokens.shape[1])
    rows_g = out_grad.reshape(N_REP, per_rep, out_grad.shape[1])
    first_new, second_new, delta = lax.map(replica_step, (rows_x, rows_g, gain, inner_weight, outer_weight, adam_m, adam_v))
    index = jnp.arange(N_REP, dtype=jnp.int32)
    offset = (1 + gossip_offset[0].astype(jnp.int32) % (N_REP - 1)).astype(jnp.int32)
    partner = ((index - offset) % N_REP).astype(jnp.int32)
    mean_delta = (delta + delta[partner]) / 2.0
    momentum_new = 0.9 * momentum + mean_delta
    outer_new = (outer_weight + outer_weight[partner]) / 2.0 - 0.7 * (0.9 * momentum_new + mean_delta)
    return (outer_new, momentum_new, first_new, second_new)
```

```python
import jax
import jax.numpy as jnp
from jax import lax
from jax.sharding import PartitionSpec as P

HEAD = 128
ADAM_STEP = 100


def from_behind(block, axis, distance):
    devices = range(lax.axis_size(axis))
    route = [((i - distance) % len(devices), i) for i in devices]
    return lax.ppermute(block, axis, route)


def gossip(values, offset, count_rep):
    def branch(distance):
        return lambda held: from_behind(held, "rep", distance)

    branches = [branch(distance) for distance in range(1, count_rep)]
    return lax.switch(offset - 1, branches, values)


def local(
    tokens, out_grad, gain, inner_weight, outer_weight, momentum, adam_m, adam_v, gossip_offset
):
    count_rep = lax.axis_size("rep")
    offset = 1 + gossip_offset[0] % (count_rep - 1)
    count_tok = tokens.shape[0]
    inner = inner_weight[0]
    outer = outer_weight[0]
    w_bf = inner.astype(jnp.bfloat16)
    outer_far = gossip(outer, offset, count_rep)
    columns = tokens
    keys = jnp.dot(
        columns,
        lax.all_gather(w_bf, "fsdp", axis=0, tiled=True),
        preferred_element_type=jnp.float32,
    )
    heads = keys.reshape(count_tok, -1, HEAD)
    scale = lax.rsqrt(jnp.mean(heads * heads, axis=-1, keepdims=True) + 1e-06)
    unit = heads * scale
    g_out = out_grad.astype(jnp.float32).reshape(heads.shape) * gain[0]
    inner_prod = jnp.mean(unit * g_out, axis=-1, keepdims=True)
    key_grad = (scale * (g_out - unit * inner_prod)).reshape(keys.shape).astype(jnp.bfloat16)
    columns = tokens
    grad = lax.psum_scatter(
        lax.dot_general(
            columns, key_grad, (((0,), (0,)), ((), ())), preferred_element_type=jnp.float32
        ),
        "fsdp",
        scatter_dimension=0,
        tiled=True,
    )
    first_new = 0.9 * adam_m[0] + 0.1 * grad
    second_new = 0.95 * adam_v[0] + 0.05 * grad * grad
    fix_one = 1.0 - 0.9**ADAM_STEP
    fix_two = 1.0 - 0.95**ADAM_STEP
    update = first_new / fix_one / (jnp.sqrt(second_new / fix_two) + 1e-08) + 0.1 * inner
    inner_next = inner - 0.05 * update
    delta = outer - inner_next
    delta_far = gossip(delta, offset, count_rep)
    mean_delta = (delta + delta_far) / 2.0
    momentum_new = 0.9 * momentum[0] + mean_delta
    outer_new = (outer + outer_far) / 2.0 - 0.7 * (0.9 * momentum_new + mean_delta)
    return (outer_new[None], momentum_new[None], first_new[None], second_new[None])


def solution(mesh):
    return jax.shard_map(
        local,
        mesh=mesh,
        in_specs=(
            P(("rep", "fsdp"), None),
            P(("rep", "fsdp"), None),
            P("rep", None),
            P("rep", "fsdp", None),
            P("rep", "fsdp", None),
            P("rep", "fsdp", None),
            P("rep", "fsdp", None),
            P("rep", "fsdp", None),
            P(),
        ),
        out_specs=(
            P("rep", "fsdp", None),
            P("rep", "fsdp", None),
            P("rep", "fsdp", None),
            P("rep", "fsdp", None),
        ),
        check_vma=False,
    )
```

```python
import jax
import jax.numpy as jnp
from jax import lax
from jax.sharding import PartitionSpec as P

HEAD = 128
ADAM_STEP = 100


def from_behind(block, axis, distance):
    devices = range(lax.axis_size(axis))
    route = [((i - distance) % len(devices), i) for i in devices]
    return lax.ppermute(block, axis, route)


def gossip(values, offset, count_rep):
    def branch(distance):
        return lambda held: from_behind(held, "rep", distance)

    branches = [branch(distance) for distance in range(1, count_rep)]
    return lax.switch(offset - 1, branches, values)


def local(
    tokens, out_grad, gain, inner_weight, outer_weight, momentum, adam_m, adam_v, gossip_offset
):
    count_rep = lax.axis_size("rep")
    offset = 1 + gossip_offset[0] % (count_rep - 1)
    count_tok = tokens.shape[0]
    inner = inner_weight[0]
    outer = outer_weight[0]
    w_bf = inner.astype(jnp.bfloat16)
    outer_far = gossip(outer, offset, count_rep)
    columns = tokens
    count_fsdp = lax.axis_size("fsdp")
    w_copies = jnp.broadcast_to(w_bf[None], (count_fsdp,) + w_bf.shape)
    w_full = lax.all_to_all(w_copies, "fsdp", 0, 0, tiled=True).reshape(-1, w_bf.shape[1])
    keys = jnp.dot(columns, w_full, preferred_element_type=jnp.float32)
    heads = keys.reshape(count_tok, -1, HEAD)
    scale = lax.rsqrt(jnp.mean(heads * heads, axis=-1, keepdims=True) + 1e-06)
    unit = heads * scale
    g_out = out_grad.astype(jnp.float32).reshape(heads.shape) * gain[0]
    inner_prod = jnp.mean(unit * g_out, axis=-1, keepdims=True)
    key_grad = (scale * (g_out - unit * inner_prod)).reshape(keys.shape).astype(jnp.bfloat16)
    columns = tokens
    grad_terms = lax.dot_general(
        columns, key_grad, (((0,), (0,)), ((), ())), preferred_element_type=jnp.float32
    )
    grad_terms = grad_terms.reshape((count_fsdp, -1) + grad_terms.shape[1:])
    grad = lax.all_to_all(grad_terms, "fsdp", 0, 0, tiled=True).sum(axis=0)
    first_new = 0.9 * adam_m[0] + 0.1 * grad
    second_new = 0.95 * adam_v[0] + 0.05 * grad * grad
    fix_one = 1.0 - 0.9**ADAM_STEP
    fix_two = 1.0 - 0.95**ADAM_STEP
    update = first_new / fix_one / (jnp.sqrt(second_new / fix_two) + 1e-08) + 0.1 * inner
    inner_next = inner - 0.05 * update
    delta = outer - inner_next
    delta_far = gossip(delta, offset, count_rep)
    mean_delta = (delta + delta_far) / 2.0
    momentum_new = 0.9 * momentum[0] + mean_delta
    outer_new = (outer + outer_far) / 2.0 - 0.7 * (0.9 * momentum_new + mean_delta)
    return (outer_new[None], momentum_new[None], first_new[None], second_new[None])


def solution(mesh):
    return jax.shard_map(
        local,
        mesh=mesh,
        in_specs=(
            P(("rep", "fsdp"), None),
            P(("rep", "fsdp"), None),
            P("rep", None),
            P("rep", "fsdp", None),
            P("rep", "fsdp", None),
            P("rep", "fsdp", None),
            P("rep", "fsdp", None),
            P("rep", "fsdp", None),
            P(),
        ),
        out_specs=(
            P("rep", "fsdp", None),
            P("rep", "fsdp", None),
            P("rep", "fsdp", None),
            P("rep", "fsdp", None),
        ),
        check_vma=False,
    )
```

```python
import jax
import jax.numpy as jnp
from jax import lax
from jax.sharding import PartitionSpec as P

HEAD = 128
ADAM_STEP = 100


def from_behind(block, axis, distance):
    devices = range(lax.axis_size(axis))
    route = [((i - distance) % len(devices), i) for i in devices]
    return lax.ppermute(block, axis, route)


def gossip(values, offset, count_rep):
    def branch(distance):
        return lambda held: from_behind(held, "rep", distance)

    branches = [branch(distance) for distance in range(1, count_rep)]
    return lax.switch(offset - 1, branches, values)


def local(
    tokens, out_grad, gain, inner_weight, outer_weight, momentum, adam_m, adam_v, gossip_offset
):
    count_rep = lax.axis_size("rep")
    offset = 1 + gossip_offset[0] % (count_rep - 1)
    count_tok = tokens.shape[0]
    inner = inner_weight[0]
    outer = outer_weight[0]
    w_bf = inner.astype(jnp.bfloat16)
    outer_far = gossip(outer, offset, count_rep)
    columns = tokens
    count_fsdp = lax.axis_size("fsdp")
    w_copies = jnp.broadcast_to(w_bf[None], (count_fsdp,) + w_bf.shape)
    w_full = lax.all_to_all(w_copies, "fsdp", 0, 0, tiled=True).reshape(-1, w_bf.shape[1])
    keys = jnp.dot(columns, w_full, preferred_element_type=jnp.float32)
    heads = keys.reshape(count_tok, -1, HEAD)
    scale = lax.rsqrt(jnp.mean(heads * heads, axis=-1, keepdims=True) + 1e-06)
    unit = heads * scale
    g_out = out_grad.astype(jnp.float32).reshape(heads.shape) * gain[0]
    inner_prod = jnp.mean(unit * g_out, axis=-1, keepdims=True)
    key_grad = (scale * (g_out - unit * inner_prod)).reshape(keys.shape).astype(jnp.bfloat16)
    columns = tokens
    grad_terms = lax.dot_general(
        columns, key_grad, (((0,), (0,)), ((), ())), preferred_element_type=jnp.float32
    )
    grad_terms = grad_terms.reshape((count_fsdp, -1) + grad_terms.shape[1:])
    grad_parts = lax.all_to_all(grad_terms.astype(jnp.bfloat16), "fsdp", 0, 0, tiled=True)
    grad = grad_parts.astype(jnp.float32).sum(axis=0)
    first_new = 0.9 * adam_m[0] + 0.1 * grad
    second_new = 0.95 * adam_v[0] + 0.05 * grad * grad
    fix_one = 1.0 - 0.9**ADAM_STEP
    fix_two = 1.0 - 0.95**ADAM_STEP
    update = first_new / fix_one / (jnp.sqrt(second_new / fix_two) + 1e-08) + 0.1 * inner
    inner_next = inner - 0.05 * update
    delta = outer - inner_next
    delta_far = gossip(delta.astype(jnp.bfloat16), offset, count_rep).astype(jnp.float32)
    mean_delta = (delta + delta_far) / 2.0
    momentum_new = 0.9 * momentum[0] + mean_delta
    outer_new = (outer + outer_far) / 2.0 - 0.7 * (0.9 * momentum_new + mean_delta)
    return (outer_new[None], momentum_new[None], first_new[None], second_new[None])


def solution(mesh):
    return jax.shard_map(
        local,
        mesh=mesh,
        in_specs=(
            P(("rep", "fsdp"), None),
            P(("rep", "fsdp"), None),
            P("rep", None),
            P("rep", "fsdp", None),
            P("rep", "fsdp", None),
            P("rep", "fsdp", None),
            P("rep", "fsdp", None),
            P("rep", "fsdp", None),
            P(),
        ),
        out_specs=(
            P("rep", "fsdp", None),
            P("rep", "fsdp", None),
            P("rep", "fsdp", None),
            P("rep", "fsdp", None),
        ),
        check_vma=False,
    )
```

```python
import jax
import jax.numpy as jnp
from jax import lax
from jax.sharding import PartitionSpec as P

HEAD = 128
ADAM_STEP = 100


def from_behind(block, axis, distance):
    devices = range(lax.axis_size(axis))
    route = [((i - distance) % len(devices), i) for i in devices]
    return lax.ppermute(block, axis, route)


def gossip(values, offset, count_rep):
    def branch(distance):
        return lambda held: from_behind(held, "rep", distance)

    branches = [branch(distance) for distance in range(1, count_rep)]
    return lax.switch(offset - 1, branches, values)


def local(
    tokens, out_grad, gain, inner_weight, outer_weight, momentum, adam_m, adam_v, gossip_offset
):
    count_rep = lax.axis_size("rep")
    offset = 1 + gossip_offset[0] % (count_rep - 1)
    count_tok = tokens.shape[0]
    inner = inner_weight[0]
    outer = outer_weight[0]
    w_bf = inner.astype(jnp.bfloat16)
    outer_far = gossip(outer, offset, count_rep)
    columns = tokens
    count_fsdp = lax.axis_size("fsdp")
    w_copies = jnp.broadcast_to(w_bf[None], (count_fsdp,) + w_bf.shape)
    w_full = lax.all_to_all(w_copies, "fsdp", 0, 0, tiled=True).reshape(-1, w_bf.shape[1])
    w_full, outer_far = lax.optimization_barrier((w_full, outer_far))
    keys = jnp.dot(columns, w_full, preferred_element_type=jnp.float32)
    heads = keys.reshape(count_tok, -1, HEAD)
    scale = lax.rsqrt(jnp.mean(heads * heads, axis=-1, keepdims=True) + 1e-06)
    unit = heads * scale
    g_out = out_grad.astype(jnp.float32).reshape(heads.shape) * gain[0]
    inner_prod = jnp.mean(unit * g_out, axis=-1, keepdims=True)
    key_grad = (scale * (g_out - unit * inner_prod)).reshape(keys.shape).astype(jnp.bfloat16)
    columns = tokens
    grad_terms = lax.dot_general(
        columns, key_grad, (((0,), (0,)), ((), ())), preferred_element_type=jnp.float32
    )
    grad_terms = grad_terms.reshape((count_fsdp, -1) + grad_terms.shape[1:])
    grad_parts = lax.all_to_all(grad_terms.astype(jnp.bfloat16), "fsdp", 0, 0, tiled=True)
    grad = grad_parts.astype(jnp.float32).sum(axis=0)
    first_new = 0.9 * adam_m[0] + 0.1 * grad
    second_new = 0.95 * adam_v[0] + 0.05 * grad * grad
    fix_one = 1.0 - 0.9**ADAM_STEP
    fix_two = 1.0 - 0.95**ADAM_STEP
    update = first_new / fix_one / (jnp.sqrt(second_new / fix_two) + 1e-08) + 0.1 * inner
    inner_next = inner - 0.05 * update
    delta = outer - inner_next
    delta_far = gossip(delta.astype(jnp.bfloat16), offset, count_rep).astype(jnp.float32)
    mean_delta = (delta + delta_far) / 2.0
    momentum_new = 0.9 * momentum[0] + mean_delta
    outer_new = (outer + outer_far) / 2.0 - 0.7 * (0.9 * momentum_new + mean_delta)
    return (outer_new[None], momentum_new[None], first_new[None], second_new[None])


def solution(mesh):
    return jax.shard_map(
        local,
        mesh=mesh,
        in_specs=(
            P(("rep", "fsdp"), None),
            P(("rep", "fsdp"), None),
            P("rep", None),
            P("rep", "fsdp", None),
            P("rep", "fsdp", None),
            P("rep", "fsdp", None),
            P("rep", "fsdp", None),
            P("rep", "fsdp", None),
            P(),
        ),
        out_specs=(
            P("rep", "fsdp", None),
            P("rep", "fsdp", None),
            P("rep", "fsdp", None),
            P("rep", "fsdp", None),
        ),
        check_vma=False,
    )
```

```python
import jax
import jax.numpy as jnp
from jax import lax
from jax.sharding import PartitionSpec as P

HEAD = 128
ADAM_STEP = 100


def from_behind(block, axis, distance):
    devices = range(lax.axis_size(axis))
    route = [((i - distance) % len(devices), i) for i in devices]
    return lax.ppermute(block, axis, route)


def gossip(values, offset, count_rep):
    def branch(distance):
        return lambda held: from_behind(held, "rep", distance)

    branches = [branch(distance) for distance in range(1, count_rep)]
    return lax.switch(offset - 1, branches, values)


def local(
    tokens, out_grad, gain, inner_weight, outer_weight, momentum, adam_m, adam_v, gossip_offset
):
    count_rep = lax.axis_size("rep")
    offset = 1 + gossip_offset[0] % (count_rep - 1)
    count_tok = tokens.shape[0]
    inner = inner_weight[0]
    outer = outer_weight[0]
    w_bf = inner.astype(jnp.bfloat16)
    columns = tokens
    count_fsdp = lax.axis_size("fsdp")
    w_copies = jnp.broadcast_to(w_bf[None], (count_fsdp,) + w_bf.shape)
    w_full = lax.all_to_all(w_copies, "fsdp", 0, 0, tiled=True).reshape(-1, w_bf.shape[1])
    keys = jnp.dot(columns, w_full, preferred_element_type=jnp.float32)
    heads = keys.reshape(count_tok, -1, HEAD)
    scale = lax.rsqrt(jnp.mean(heads * heads, axis=-1, keepdims=True) + 1e-06)
    unit = heads * scale
    g_out = out_grad.astype(jnp.float32).reshape(heads.shape) * gain[0]
    inner_prod = jnp.mean(unit * g_out, axis=-1, keepdims=True)
    key_grad = (scale * (g_out - unit * inner_prod)).reshape(keys.shape).astype(jnp.bfloat16)
    columns = tokens
    grad_terms = lax.dot_general(
        columns, key_grad, (((0,), (0,)), ((), ())), preferred_element_type=jnp.float32
    )
    grad_terms = grad_terms.reshape((count_fsdp, -1) + grad_terms.shape[1:])
    grad_parts = lax.all_to_all(grad_terms.astype(jnp.bfloat16), "fsdp", 0, 0, tiled=True)
    grad = grad_parts.astype(jnp.float32).sum(axis=0)
    first_new = 0.9 * adam_m[0] + 0.1 * grad
    second_new = 0.95 * adam_v[0] + 0.05 * grad * grad
    fix_one = 1.0 - 0.9**ADAM_STEP
    fix_two = 1.0 - 0.95**ADAM_STEP
    update = first_new / fix_one / (jnp.sqrt(second_new / fix_two) + 1e-08) + 0.1 * inner
    inner_next = inner - 0.05 * update
    delta = outer - inner_next
    outer_hi = outer.astype(jnp.bfloat16)
    outer_lo = (outer - outer_hi.astype(jnp.float32)).astype(jnp.bfloat16)
    sent = jnp.stack([outer_hi, outer_lo, delta.astype(jnp.bfloat16)])
    far = gossip(sent, offset, count_rep).astype(jnp.float32)
    outer_far = far[0] + far[1]
    delta_far = far[2]
    mean_delta = (delta + delta_far) / 2.0
    momentum_new = 0.9 * momentum[0] + mean_delta
    outer_new = (outer + outer_far) / 2.0 - 0.7 * (0.9 * momentum_new + mean_delta)
    return (outer_new[None], momentum_new[None], first_new[None], second_new[None])


def solution(mesh):
    return jax.shard_map(
        local,
        mesh=mesh,
        in_specs=(
            P(("rep", "fsdp"), None),
            P(("rep", "fsdp"), None),
            P("rep", None),
            P("rep", "fsdp", None),
            P("rep", "fsdp", None),
            P("rep", "fsdp", None),
            P("rep", "fsdp", None),
            P("rep", "fsdp", None),
            P(),
        ),
        out_specs=(
            P("rep", "fsdp", None),
            P("rep", "fsdp", None),
            P("rep", "fsdp", None),
            P("rep", "fsdp", None),
        ),
        check_vma=False,
    )
```

```python
import jax
import jax.numpy as jnp
from jax import lax
from jax.experimental.layout import Layout, with_layout_constraint
from jax.sharding import PartitionSpec as P

HEAD = 128
ADAM_STEP = 100


def from_behind(block, axis, distance):
    devices = range(lax.axis_size(axis))
    route = [((i - distance) % len(devices), i) for i in devices]
    return lax.ppermute(block, axis, route)


def gossip(values, offset, count_rep):
    def branch(distance):
        return lambda held: from_behind(held, "rep", distance)

    branches = [branch(distance) for distance in range(1, count_rep)]
    return lax.switch(offset - 1, branches, values)


def local(
    tokens, out_grad, gain, inner_weight, outer_weight, momentum, adam_m, adam_v, gossip_offset
):
    count_rep = lax.axis_size("rep")
    offset = 1 + gossip_offset[0] % (count_rep - 1)
    count_tok = tokens.shape[0]
    inner = inner_weight[0]
    outer = outer_weight[0]
    w_bf = inner.astype(jnp.bfloat16)
    columns = tokens
    count_fsdp = lax.axis_size("fsdp")
    w_copies = jnp.broadcast_to(w_bf[None], (count_fsdp,) + w_bf.shape)
    w_pieces = lax.all_to_all(w_copies, "fsdp", 0, 0, tiled=True)
    columns = tokens.reshape(count_tok, count_fsdp, -1)
    keys = lax.dot_general(
        columns, w_pieces, (((1, 2), (0, 1)), ((), ())), preferred_element_type=jnp.float32
    )
    heads = keys.reshape(count_tok, -1, HEAD)
    scale = lax.rsqrt(jnp.mean(heads * heads, axis=-1, keepdims=True) + 1e-06)
    unit = heads * scale
    g_out = out_grad.astype(jnp.float32).reshape(heads.shape) * gain[0]
    inner_prod = jnp.mean(unit * g_out, axis=-1, keepdims=True)
    key_grad = (scale * (g_out - unit * inner_prod)).reshape(keys.shape).astype(jnp.bfloat16)
    grad_terms = lax.dot_general(
        columns, key_grad, (((0,), (0,)), ((), ())), preferred_element_type=jnp.float32
    )
    grad_parts = lax.all_to_all(grad_terms.astype(jnp.bfloat16), "fsdp", 0, 0, tiled=True)
    grad = grad_parts.astype(jnp.float32).sum(axis=0)
    grad = with_layout_constraint(grad, Layout((0, 1)))
    first_new = 0.9 * adam_m[0] + 0.1 * grad
    second_new = 0.95 * adam_v[0] + 0.05 * grad * grad
    fix_one = 1.0 - 0.9**ADAM_STEP
    fix_two = 1.0 - 0.95**ADAM_STEP
    update = first_new / fix_one / (jnp.sqrt(second_new / fix_two) + 1e-08) + 0.1 * inner
    inner_next = inner - 0.05 * update
    delta = outer - inner_next
    outer_hi = outer.astype(jnp.bfloat16)
    outer_lo = (outer - outer_hi.astype(jnp.float32)).astype(jnp.bfloat16)
    sent = jnp.stack([outer_hi, outer_lo, delta.astype(jnp.bfloat16)])
    far = gossip(sent, offset, count_rep).astype(jnp.float32)
    outer_far = far[0] + far[1]
    delta_far = far[2]
    mean_delta = (delta + delta_far) / 2.0
    momentum_new = 0.9 * momentum[0] + mean_delta
    outer_new = (outer + outer_far) / 2.0 - 0.7 * (0.9 * momentum_new + mean_delta)
    return (outer_new[None], momentum_new[None], first_new[None], second_new[None])


def solution(mesh):
    return jax.shard_map(
        local,
        mesh=mesh,
        in_specs=(
            P(("rep", "fsdp"), None),
            P(("rep", "fsdp"), None),
            P("rep", None),
            P("rep", "fsdp", None),
            P("rep", "fsdp", None),
            P("rep", "fsdp", None),
            P("rep", "fsdp", None),
            P("rep", "fsdp", None),
            P(),
        ),
        out_specs=(
            P("rep", "fsdp", None),
            P("rep", "fsdp", None),
            P("rep", "fsdp", None),
            P("rep", "fsdp", None),
        ),
        check_vma=False,
    )
```

```python
import jax
import jax.numpy as jnp
from jax import lax
from jax.experimental.layout import Layout, with_layout_constraint
from jax.sharding import PartitionSpec as P

HEAD = 128
ADAM_STEP = 100


def from_behind(block, axis, distance):
    devices = range(lax.axis_size(axis))
    route = [((i - distance) % len(devices), i) for i in devices]
    return lax.ppermute(block, axis, route)


def gossip(values, offset, count_rep):
    def branch(distance):
        return lambda held: from_behind(held, "rep", distance)

    branches = [branch(distance) for distance in range(1, count_rep)]
    return lax.switch(offset - 1, branches, values)


def local(
    tokens, out_grad, gain, inner_weight, outer_weight, momentum, adam_m, adam_v, gossip_offset
):
    count_rep = lax.axis_size("rep")
    offset = 1 + gossip_offset[0] % (count_rep - 1)
    count_tok = tokens.shape[0]
    inner = inner_weight[0]
    outer = outer_weight[0]
    w_bf = inner.astype(jnp.bfloat16)
    columns = tokens
    count_fsdp = lax.axis_size("fsdp")
    w_copies = jnp.broadcast_to(w_bf[None], (count_fsdp,) + w_bf.shape)
    w_pieces = lax.all_to_all(w_copies, "fsdp", 0, 0, tiled=True)
    columns = tokens.reshape(count_tok, count_fsdp, -1)
    keys = lax.dot_general(
        columns, w_pieces, (((1, 2), (0, 1)), ((), ())), preferred_element_type=jnp.float32
    )
    heads = keys.reshape(count_tok, -1, HEAD)
    scale = lax.rsqrt(jnp.mean(heads * heads, axis=-1, keepdims=True) + 1e-06)
    unit = heads * scale
    g_out = out_grad.astype(jnp.float32).reshape(heads.shape) * gain[0]
    inner_prod = jnp.mean(unit * g_out, axis=-1, keepdims=True)
    key_grad = (scale * (g_out - unit * inner_prod)).reshape(keys.shape).astype(jnp.bfloat16)
    grad_terms = lax.dot_general(
        columns, key_grad, (((0,), (0,)), ((), ())), preferred_element_type=jnp.float32
    )
    grad_parts = lax.all_to_all(grad_terms.astype(jnp.bfloat16), "fsdp", 0, 0, tiled=True)
    grad = grad_parts.astype(jnp.float32).sum(axis=0)
    grad = with_layout_constraint(grad, Layout((0, 1)))
    first_new = 0.9 * adam_m[0] + 0.1 * grad
    second_new = 0.95 * adam_v[0] + 0.05 * grad * grad
    fix_one = 1.0 - 0.9**ADAM_STEP
    fix_two = 1.0 - 0.95**ADAM_STEP
    update = first_new / fix_one / (jnp.sqrt(second_new / fix_two) + 1e-08) + 0.1 * inner
    inner_next = inner - 0.05 * update
    delta = outer - inner_next
    sent = jnp.stack([outer, delta]).astype(jnp.bfloat16)
    far = gossip(sent, offset, count_rep).astype(jnp.float32)
    outer_far = far[0]
    delta_far = far[1]
    mean_delta = (delta + delta_far) / 2.0
    momentum_new = 0.9 * momentum[0] + mean_delta
    outer_new = (outer + outer_far) / 2.0 - 0.7 * (0.9 * momentum_new + mean_delta)
    return (outer_new[None], momentum_new[None], first_new[None], second_new[None])


def solution(mesh):
    return jax.shard_map(
        local,
        mesh=mesh,
        in_specs=(
            P(("rep", "fsdp"), None),
            P(("rep", "fsdp"), None),
            P("rep", None),
            P("rep", "fsdp", None),
            P("rep", "fsdp", None),
            P("rep", "fsdp", None),
            P("rep", "fsdp", None),
            P("rep", "fsdp", None),
            P(),
        ),
        out_specs=(
            P("rep", "fsdp", None),
            P("rep", "fsdp", None),
            P("rep", "fsdp", None),
            P("rep", "fsdp", None),
        ),
        check_vma=False,
    )
```

```python
import jax
import jax.numpy as jnp
from jax import lax
from jax.experimental.layout import Layout, with_layout_constraint
from jax.sharding import Mesh, PartitionSpec as P

HEAD = 128
ADAM_STEP = 100


def from_behind(block, axis, distance):
    devices = range(lax.axis_size(axis))
    route = [((i - distance) % len(devices), i) for i in devices]
    return lax.ppermute(block, axis, route)


def gossip(values, offset, count_rep):
    def branch(distance):
        return lambda held: from_behind(held, "rep", distance)

    branches = [branch(distance) for distance in range(1, count_rep)]
    return lax.switch(offset - 1, branches, values)


def local(
    tokens, out_grad, gain, inner_weight, outer_weight, momentum, adam_m, adam_v, gossip_offset
):
    count_rep = lax.axis_size("rep")
    offset = 1 + gossip_offset[0] % (count_rep - 1)
    count_tok = tokens.shape[0]
    inner = inner_weight[0]
    outer = outer_weight[0]
    w_bf = inner.astype(jnp.bfloat16)
    columns = tokens
    count_far = lax.axis_size("far")
    count_near = lax.axis_size("near")
    count_fsdp = count_far * count_near
    w_pair = lax.all_to_all(
        jnp.broadcast_to(w_bf[None], (count_far,) + w_bf.shape), "far", 0, 0, tiled=True
    )
    w_pieces = lax.all_to_all(
        jnp.broadcast_to(w_pair[None], (count_near,) + w_pair.shape), "near", 0, 0, tiled=True
    )
    columns = tokens.reshape(count_tok, count_far, count_near, -1)
    keys = lax.dot_general(
        columns, w_pieces, (((1, 2, 3), (1, 0, 2)), ((), ())), preferred_element_type=jnp.float32
    )
    columns = tokens.reshape(count_tok, count_fsdp, -1)
    heads = keys.reshape(count_tok, -1, HEAD)
    scale = lax.rsqrt(jnp.mean(heads * heads, axis=-1, keepdims=True) + 1e-06)
    unit = heads * scale
    g_out = out_grad.astype(jnp.float32).reshape(heads.shape) * gain[0]
    inner_prod = jnp.mean(unit * g_out, axis=-1, keepdims=True)
    key_grad = (scale * (g_out - unit * inner_prod)).reshape(keys.shape).astype(jnp.bfloat16)
    grad_terms = lax.dot_general(
        columns, key_grad, (((0,), (0,)), ((), ())), preferred_element_type=jnp.float32
    )
    grad_parts = lax.all_to_all(
        grad_terms.astype(jnp.bfloat16), ("far", "near"), 0, 0, tiled=True
    )
    grad = grad_parts.astype(jnp.float32).sum(axis=0)
    grad = with_layout_constraint(grad, Layout((0, 1)))
    first_new = 0.9 * adam_m[0] + 0.1 * grad
    second_new = 0.95 * adam_v[0] + 0.05 * grad * grad
    fix_one = 1.0 - 0.9**ADAM_STEP
    fix_two = 1.0 - 0.95**ADAM_STEP
    update = first_new / fix_one / (jnp.sqrt(second_new / fix_two) + 1e-08) + 0.1 * inner
    inner_next = inner - 0.05 * update
    delta = outer - inner_next
    sent = jnp.stack([outer, delta]).astype(jnp.bfloat16)
    far = gossip(sent, offset, count_rep).astype(jnp.float32)
    outer_far = far[0]
    delta_far = far[1]
    mean_delta = (delta + delta_far) / 2.0
    momentum_new = 0.9 * momentum[0] + mean_delta
    outer_new = (outer + outer_far) / 2.0 - 0.7 * (0.9 * momentum_new + mean_delta)
    return (outer_new[None], momentum_new[None], first_new[None], second_new[None])


def split_fsdp(mesh):
    devices = mesh.devices
    rows = {device.coords[1] for device in devices[0]}
    count_far = len(rows)
    shape = (devices.shape[0], count_far, devices.shape[1] // count_far)
    return Mesh(devices.reshape(shape), ("rep", "far", "near"))


def solution(mesh):
    fsdp = ("far", "near")
    weights = P("rep", fsdp, None)
    return jax.shard_map(
        local,
        mesh=split_fsdp(mesh),
        in_specs=(
            P(("rep",) + fsdp, None),
            P(("rep",) + fsdp, None),
            P("rep", None),
            weights,
            weights,
            weights,
            weights,
            weights,
            P(),
        ),
        out_specs=(weights, weights, weights, weights),
        check_vma=False,
    )
```

```python
import jax
import jax.numpy as jnp
from jax import lax
from jax.experimental.layout import Layout, with_layout_constraint
from jax.sharding import PartitionSpec as P

HEAD = 128
ADAM_STEP = 100


def from_behind(block, axis, distance):
    devices = range(lax.axis_size(axis))
    route = [((i - distance) % len(devices), i) for i in devices]
    return lax.ppermute(block, axis, route)


def gossip(values, offset, count_rep):
    def branch(distance):
        return lambda held: from_behind(held, "rep", distance)

    branches = [branch(distance) for distance in range(1, count_rep)]
    return lax.switch(offset - 1, branches, values)


def local(
    tokens, out_grad, gain, inner_weight, outer_weight, momentum, adam_m, adam_v, gossip_offset
):
    count_rep = lax.axis_size("rep")
    offset = 1 + gossip_offset[0] % (count_rep - 1)
    count_tok = tokens.shape[0]
    inner = inner_weight[0]
    outer = outer_weight[0]
    w_bf = inner.astype(jnp.bfloat16)
    columns = tokens
    count_fsdp = lax.axis_size("fsdp")
    w_copies = jnp.broadcast_to(w_bf[None], (count_fsdp,) + w_bf.shape)
    w_pieces = lax.all_to_all(w_copies, "fsdp", 0, 0, tiled=True)
    columns = tokens.reshape(count_tok, count_fsdp, -1)
    keys = lax.dot_general(
        columns, w_pieces, (((1, 2), (0, 1)), ((), ())), preferred_element_type=jnp.float32
    )
    heads = keys.reshape(count_tok, -1, HEAD)
    scale = lax.rsqrt(jnp.mean(heads * heads, axis=-1, keepdims=True) + 1e-06)
    unit = heads * scale
    g_out = out_grad.astype(jnp.float32).reshape(heads.shape) * gain[0]
    inner_prod = jnp.mean(unit * g_out, axis=-1, keepdims=True)
    key_grad = (scale * (g_out - unit * inner_prod)).reshape(keys.shape).astype(jnp.bfloat16)
    grad_terms = lax.dot_general(
        columns, key_grad, (((0,), (0,)), ((), ())), preferred_element_type=jnp.float32
    )
    grad_parts = lax.all_to_all(grad_terms.astype(jnp.bfloat16), "fsdp", 0, 0, tiled=True)
    grad = grad_parts.astype(jnp.float32).sum(axis=0)
    grad = with_layout_constraint(grad, Layout((0, 1)))
    first_new = 0.9 * adam_m[0] + 0.1 * grad
    second_new = 0.95 * adam_v[0] + 0.05 * grad * grad
    fix_one = 1.0 - 0.9**ADAM_STEP
    fix_two = 1.0 - 0.95**ADAM_STEP
    update = first_new / fix_one / (jnp.sqrt(second_new / fix_two) + 1e-08) + 0.1 * inner
    inner_next = inner - 0.05 * update
    delta = outer - inner_next
    sent = jnp.stack([outer, delta]).astype(jnp.bfloat16)
    far = gossip(sent, offset, count_rep)
    outer_far = far[0]
    delta_far = far[1]
    mean_delta = (delta + delta_far) / 2.0
    momentum_new = 0.9 * momentum[0] + mean_delta
    outer_new = (outer + outer_far) / 2.0 - 0.7 * (0.9 * momentum_new + mean_delta)
    return (outer_new[None], momentum_new[None], first_new[None], second_new[None])


def solution(mesh):
    return jax.shard_map(
        local,
        mesh=mesh,
        in_specs=(
            P(("rep", "fsdp"), None),
            P(("rep", "fsdp"), None),
            P("rep", None),
            P("rep", "fsdp", None),
            P("rep", "fsdp", None),
            P("rep", "fsdp", None),
            P("rep", "fsdp", None),
            P("rep", "fsdp", None),
            P(),
        ),
        out_specs=(
            P("rep", "fsdp", None),
            P("rep", "fsdp", None),
            P("rep", "fsdp", None),
            P("rep", "fsdp", None),
        ),
        check_vma=False,
    )
```

```python
import jax
import jax.numpy as jnp
from jax import lax
from jax.experimental.layout import Layout, with_layout_constraint
from jax.sharding import PartitionSpec as P

HEAD = 128
ADAM_STEP = 100


def mirror(block, axis, centre):
    devices = range(lax.axis_size(axis))
    route = [(i, (centre - i) % len(devices)) for i in devices]
    return lax.ppermute(block, axis, route)


def gossip(values, offset, count_rep):
    def branch(distance):
        return lambda held: mirror(held, "rep", count_rep - 1 + distance)

    mirrored = mirror(values, "rep", count_rep - 1)
    branches = [branch(distance) for distance in range(1, count_rep)]
    return lax.switch(offset - 1, branches, mirrored)


def local(
    tokens, out_grad, gain, inner_weight, outer_weight, momentum, adam_m, adam_v, gossip_offset
):
    count_rep = lax.axis_size("rep")
    offset = 1 + gossip_offset[0] % (count_rep - 1)
    count_tok = tokens.shape[0]
    inner = inner_weight[0]
    outer = outer_weight[0]
    w_bf = inner.astype(jnp.bfloat16)
    columns = tokens
    count_fsdp = lax.axis_size("fsdp")
    w_copies = jnp.broadcast_to(w_bf[None], (count_fsdp,) + w_bf.shape)
    w_pieces = lax.all_to_all(w_copies, "fsdp", 0, 0, tiled=True)
    columns = tokens.reshape(count_tok, count_fsdp, -1)
    keys = lax.dot_general(
        columns, w_pieces, (((1, 2), (0, 1)), ((), ())), preferred_element_type=jnp.float32
    )
    heads = keys.reshape(count_tok, -1, HEAD)
    scale = lax.rsqrt(jnp.mean(heads * heads, axis=-1, keepdims=True) + 1e-06)
    unit = heads * scale
    g_out = out_grad.astype(jnp.float32).reshape(heads.shape) * gain[0]
    inner_prod = jnp.mean(unit * g_out, axis=-1, keepdims=True)
    key_grad = (scale * (g_out - unit * inner_prod)).reshape(keys.shape).astype(jnp.bfloat16)
    grad_terms = lax.dot_general(
        columns, key_grad, (((0,), (0,)), ((), ())), preferred_element_type=jnp.float32
    )
    grad_parts = lax.all_to_all(grad_terms.astype(jnp.bfloat16), "fsdp", 0, 0, tiled=True)
    grad = grad_parts.astype(jnp.float32).sum(axis=0)
    grad = with_layout_constraint(grad, Layout((0, 1)))
    first_new = 0.9 * adam_m[0] + 0.1 * grad
    second_new = 0.95 * adam_v[0] + 0.05 * grad * grad
    fix_one = 1.0 - 0.9**ADAM_STEP
    fix_two = 1.0 - 0.95**ADAM_STEP
    update = first_new / fix_one / (jnp.sqrt(second_new / fix_two) + 1e-08) + 0.1 * inner
    inner_next = inner - 0.05 * update
    delta = outer - inner_next
    sent = jnp.stack([outer, delta]).astype(jnp.bfloat16)
    far = gossip(sent, offset, count_rep)
    outer_far = far[0]
    delta_far = far[1]
    mean_delta = (delta + delta_far) / 2.0
    momentum_new = 0.9 * momentum[0] + mean_delta
    outer_new = (outer + outer_far) / 2.0 - 0.7 * (0.9 * momentum_new + mean_delta)
    return (outer_new[None], momentum_new[None], first_new[None], second_new[None])


def solution(mesh):
    return jax.shard_map(
        local,
        mesh=mesh,
        in_specs=(
            P(("rep", "fsdp"), None),
            P(("rep", "fsdp"), None),
            P("rep", None),
            P("rep", "fsdp", None),
            P("rep", "fsdp", None),
            P("rep", "fsdp", None),
            P("rep", "fsdp", None),
            P("rep", "fsdp", None),
            P(),
        ),
        out_specs=(
            P("rep", "fsdp", None),
            P("rep", "fsdp", None),
            P("rep", "fsdp", None),
            P("rep", "fsdp", None),
        ),
        check_vma=False,
    )
```

```python
import jax
import jax.numpy as jnp
from jax import lax
from jax.experimental.layout import Layout, with_layout_constraint
from jax.sharding import Mesh, PartitionSpec as P

HEAD = 128
ADAM_STEP = 100


def from_behind(block, axis, distance):
    devices = range(lax.axis_size(axis))
    route = [((i - distance) % len(devices), i) for i in devices]
    return lax.ppermute(block, axis, route)


def gossip(values, offset, count_rep):
    def branch(distance):
        return lambda held: from_behind(held, "rep", distance)

    branches = [branch(distance) for distance in range(1, count_rep)]
    return lax.switch(offset - 1, branches, values)


def local(
    tokens, out_grad, gain, inner_weight, outer_weight, momentum, adam_m, adam_v, gossip_offset
):
    count_rep = lax.axis_size("rep")
    offset = 1 + gossip_offset[0] % (count_rep - 1)
    count_tok = tokens.shape[0]
    inner = inner_weight[0]
    outer = outer_weight[0]
    w_bf = inner.astype(jnp.bfloat16)
    columns = tokens
    count_far = lax.axis_size("far")
    count_near = lax.axis_size("near")
    count_fsdp = count_far * count_near
    w_pair = lax.all_to_all(
        jnp.broadcast_to(w_bf[None], (count_far,) + w_bf.shape), "far", 0, 0, tiled=True
    )
    w_pieces = lax.all_to_all(
        jnp.broadcast_to(w_pair[None], (count_near,) + w_pair.shape), "near", 0, 0, tiled=True
    )
    columns = tokens.reshape(count_tok, count_far, count_near, -1)
    keys = lax.dot_general(
        columns, w_pieces, (((1, 2, 3), (1, 0, 2)), ((), ())), preferred_element_type=jnp.float32
    )
    columns = tokens.reshape(count_tok, count_fsdp, -1)
    heads = keys.reshape(count_tok, -1, HEAD)
    scale = lax.rsqrt(jnp.mean(heads * heads, axis=-1, keepdims=True) + 1e-06)
    unit = heads * scale
    g_out = out_grad.astype(jnp.float32).reshape(heads.shape) * gain[0]
    inner_prod = jnp.mean(unit * g_out, axis=-1, keepdims=True)
    key_grad = (scale * (g_out - unit * inner_prod)).reshape(keys.shape).astype(jnp.bfloat16)
    grad_terms = lax.dot_general(
        columns, key_grad, (((0,), (0,)), ((), ())), preferred_element_type=jnp.float32
    )
    grad_parts = lax.all_to_all(
        grad_terms.astype(jnp.bfloat16), ("far", "near"), 0, 0, tiled=True
    )
    grad = grad_parts.astype(jnp.float32).sum(axis=0)
    grad = with_layout_constraint(grad, Layout((0, 1)))
    first_new = 0.9 * adam_m[0] + 0.1 * grad
    second_new = 0.95 * adam_v[0] + 0.05 * grad * grad
    fix_one = 1.0 - 0.9**ADAM_STEP
    fix_two = 1.0 - 0.95**ADAM_STEP
    update = first_new / fix_one / (jnp.sqrt(second_new / fix_two) + 1e-08) + 0.1 * inner
    inner_next = inner - 0.05 * update
    delta = outer - inner_next
    sent = jnp.stack([outer, delta]).astype(jnp.bfloat16)
    far = gossip(sent, offset, count_rep)
    outer_far = far[0]
    delta_far = far[1]
    mean_delta = (delta + delta_far) / 2.0
    momentum_new = 0.9 * momentum[0] + mean_delta
    outer_new = (outer + outer_far) / 2.0 - 0.7 * (0.9 * momentum_new + mean_delta)
    return (outer_new[None], momentum_new[None], first_new[None], second_new[None])


def split_fsdp(mesh):
    devices = mesh.devices
    rows = {device.coords[1] for device in devices[0]}
    count_far = len(rows)
    shape = (devices.shape[0], count_far, devices.shape[1] // count_far)
    return Mesh(devices.reshape(shape), ("rep", "far", "near"))


def solution(mesh):
    fsdp = ("far", "near")
    weights = P("rep", fsdp, None)
    return jax.shard_map(
        local,
        mesh=split_fsdp(mesh),
        in_specs=(
            P(("rep",) + fsdp, None),
            P(("rep",) + fsdp, None),
            P("rep", None),
            weights,
            weights,
            weights,
            weights,
            weights,
            P(),
        ),
        out_specs=(weights, weights, weights, weights),
        check_vma=False,
    )
```
